256 devices in a mesh: eg: 16 (over x_hi, z), blk: 16 (over x_lo, y, core).
Axes of the slice: x: 4 (x_hi: 2, x_lo: 2; x = x_hi * 2 + x_lo), y: 4, z: 8, core: 2. Of those that a mesh axis runs over, the one named last changes fastest.
Arguments:
- tokens: bfloat16 [2048, 7168], P(('eg', 'blk')), may hold values from -6 to 6
- grad_out: bfloat16 [2048, 7168], P(('eg', 'blk')), may hold values from -4 to 4
- expert_ids: int32 [2048, 2], P(('eg', 'blk')), may hold values from 0 to 15, all different within a row; in each aligned block of 8 rows (0 to 7, 8 to 15, ...) at most 2 rows name the same one
- gate_weights: bfloat16 [2048, 2], P(('eg', 'blk')), may hold values from 0.049804688 to 1
- gate_codes: bfloat16 [16, 7168, 2048], P('eg', None, 'blk'), may hold values from -0.0625 to 0.0625
- up_codes: bfloat16 [16, 7168, 2048], P('eg', None, 'blk'), may hold values from -0.0625 to 0.0625
- down_codes: bfloat16 [16, 7168, 2048], P('eg', None, 'blk'), may hold values from -0.125 to 0.125
- block_scales: bfloat16 [16, 3, 16, 56], P('eg', None, 'blk'), may hold values from 0.29882812 to 3
Outputs:
- grad_tokens: bfloat16 [2048, 7168], P(('eg', 'blk'))
- grad_gates: bfloat16 [2048, 2], P(('eg', 'blk'))
- gate_grad: bfloat16 [16, 7168, 2048], P('eg', None, 'blk')
- up_grad: bfloat16 [16, 7168, 2048], P('eg', None, 'blk')
- down_grad: bfloat16 [16, 7168, 2048], P('eg', None, 'blk')
The draws below stay inside these ranges and needn't reach their ends.
Inputs may be any that keep to these rules, and one draw needn't show every extreme that they name: `expert_ids`: each token names 2 different experts. Among the 8 tokens of one device (aligned blocks of rows) at most 2 name the same expert, and in every draw some device's tokens reach 2 for some expert.
All inputs are finite; a program needn't handle non-finite values.
Results may differ from the reference program's by a relative error of at most 0.028.
Values may be sent and summed in bfloat16 or wider, within the bound.
No kernel may reach another device: no remote copies, remote signals or barrier semaphores. Data moves between devices by JAX's collectives and lax.ppermute only.
A program may use at most 128 MiB of HBM per device.

```python
import math
import jax
import jax.numpy as jnp
import numpy as np
from jax import lax

D = 7168
HID = 2048
QBLOCK = 128
TOPK = 2
TOK_DEV = 8
EXPERTS = 16
CAP = 2
TOKENS = 2048
N_EG = 16
N_BLK = 16


def shard_levels(stream_key, extent, pieces, least, top_value):
    factor_of = 1.0
    for dim, shards_of in pieces:
        steps = jax.random.uniform(jax.random.fold_in(jax.random.fold_in(stream_key, 6), dim), (shards_of,), jnp.float32, least / len(pieces), top_value / len(pieces))
        factor_of = factor_of * jnp.repeat(jnp.exp(steps), extent[dim] // shards_of).reshape((-1,) + (1,) * (len(extent) - 1 - dim))
    return factor_of


def assign_block(own_key, own, number, rows, amount, top, bound, slope):
    order = jax.random.permutation(own_key, amount)
    crowded, common = portions_of(amount, rows * top, bound, slope, True), portions_of(amount, rows * top, bound, slope, False)
    places = jnp.arange(amount)

    def named(sizes, rotation):
        used = int((sizes > 0).sum())
        fixed = max(1, used // 4)
        shifted = fixed + (places - fixed + rotation * (used - fixed)) % max(1, amount - fixed)
        return jnp.zeros((amount,), jnp.int32).at[order[jnp.where(places < fixed, places, shifted)]].set(jnp.asarray(sizes, jnp.int32))

    sizes = jnp.where(number % 4 == 0, named(crowded, number // 4), named(common, number - number // 4 - 1))
    mixed = jax.random.permutation(jax.random.fold_in(own, 3), amount)
    donor, sink = mixed[0:amount // 2 * 2:2], mixed[1:amount // 2 * 2:2]
    margin = jnp.minimum(sizes[donor] - 1, bound - sizes[sink]) // 2
    margin = jnp.where((donor == order[0]) | (sink == order[0]) | (sizes[sink] == 0), 0, jnp.maximum(margin, 0))
    shifted = jax.random.randint(jax.random.fold_in(own, 4), (amount // 2,), 0, 1 << 20) % (margin + 1)
    sizes = sizes.at[donor].add(-shifted).at[sink].add(shifted)
    labels = jnp.searchsorted(jnp.cumsum(sizes), jnp.arange(rows * top), side="right").astype(jnp.int32)
    listing = labels.reshape(top, rows).T
    listing = listing[jax.random.permutation(jax.random.fold_in(own, 1), rows)]
    rotation = jax.random.randint(jax.random.fold_in(own, 2), (rows, 1), 0, top)
    return jnp.take_along_axis(listing, (jnp.arange(top)[None, :] + rotation) % top, axis=1)


def portions_of(amount, total, limit, skew, full):
    loads = [(1 << 20) // math.isqrt(standing ** skew) + 1 for standing in range(1, amount + 1)]
    largest = limit if full else min(limit, max(-(-total // amount), total * loads[0] // sum(loads)))
    least = 1 if total - largest >= amount - 1 else 0
    given, rest = [largest] + [least] * (amount - 1), total - largest - least * (amount - 1)
    while rest > 0:
        free = [i for i in range(1, amount) if given[i] < largest] or [i for i in range(1, amount) if given[i] < limit]
        mass, budget = sum([loads[i] for i in free]), rest
        for i in free:
            addition = min(limit - given[i], max(1, budget * loads[i] // mass), rest)
            given[i] = given[i] + addition
            rest = rest - addition
    return np.array(given)


def normal_values(stream_key, dims, scale, reach, shards=(), held_as=jnp.bfloat16):
    array = scale * jax.random.normal(stream_key, dims, jnp.float32)
    if shards:
        array = array * shard_levels(stream_key, dims, shards, -0.22, 0.18)
    return jnp.clip(array, -reach, reach).astype(held_as)


def setup_inputs(seed: int = 0) -> dict:
    seeds = jax.random.split(jax.random.key(seed), 9)
    tokens = normal_values(seeds[0], (TOKENS, D), 1.0, 6.0, ((0, 256),))
    grad_out = normal_values(seeds[1], (TOKENS, D), 0.5, 4.0, ((0, 256),))
    expert_ids_keys = jax.random.split(jax.random.fold_in(seeds[2], 1), TOKENS // TOK_DEV)
    expert_ids_turns = jax.random.permutation(jax.random.fold_in(seeds[2], 3), TOKENS // TOK_DEV)
    expert_ids = jax.vmap(lambda own, number: assign_block(jax.random.fold_in(seeds[2], 2), own, number, TOK_DEV, EXPERTS, TOPK, CAP, 2))(expert_ids_keys, expert_ids_turns).reshape((TOKENS, TOPK))
    gate_weights = jnp.clip(jnp.exp(math.log(1.0) - 2.9996462 * jax.random.uniform(seeds[3], (TOKENS, TOPK), jnp.float32) ** shard_levels(seeds[3], (TOKENS, TOPK), ((0, 256),), -0.2, 0.2)), 0.049804688, 1.0).astype(jnp.bfloat16)
    gate_codes = normal_values(seeds[4], (EXPERTS, D, HID), D ** -0.5, 0.0625, ((0, 16), (2, 16)))
    up_codes = normal_values(seeds[5], (EXPERTS, D, HID), D ** -0.5, 0.0625, ((0, 16), (2, 16)))
    down_codes = normal_values(seeds[6], (EXPERTS, D, HID), HID ** -0.5, 0.125, ((0, 16), (2, 16)))
    block_scales = jnp.clip(jnp.exp(math.log(3.0) - 2.306499 * jax.random.uniform(seeds[7], (EXPERTS, 3, HID // QBLOCK, D // QBLOCK), jnp.float32) ** shard_levels(seeds[7], (EXPERTS, 3, HID // QBLOCK, D // QBLOCK), ((0, 16), (2, 16)), -0.2, 0.2)), 0.29882812, 3.0).astype(jnp.bfloat16)
    return dict(tokens=tokens, grad_out=grad_out, expert_ids=expert_ids, gate_weights=gate_weights, gate_codes=gate_codes, up_codes=up_codes, down_codes=down_codes, block_scales=block_scales)


def dequantize(codes, scales):
    rows_in, cols_in = codes.shape
    blocks = codes.astype(jnp.float32).reshape(rows_in // QBLOCK, QBLOCK, cols_in // QBLOCK, QBLOCK)
    scaled = blocks * jnp.transpose(scales.astype(jnp.float32))[:, None, :, None]
    return scaled.reshape(rows_in, cols_in).astype(jnp.bfloat16)


def backward_math(gate_pre, up_pre, down_back, gates):
    sigma = jax.nn.sigmoid(gate_pre)
    hidden = gate_pre * sigma * up_pre
    grad_hidden = gates[:, None] * down_back
    grad_up = (grad_hidden * gate_pre * sigma).astype(jnp.bfloat16)
    grad_gate = (grad_hidden * up_pre * sigma * (1.0 + gate_pre * (1.0 - sigma))).astype(jnp.bfloat16)
    gated_hidden = (gates[:, None] * hidden).astype(jnp.bfloat16)
    return hidden, grad_gate, grad_up, gated_hidden


def reference(tokens, grad_out, expert_ids, gate_weights, gate_codes, up_codes, down_codes, block_scales):
    span = N_EG * N_BLK * CAP
    width = tokens.shape[1]
    flat = expert_ids.reshape(-1).astype(jnp.int32)
    order = jnp.argsort(flat, stable=True).astype(jnp.int32)
    counts = jnp.sum((flat[:, None] == jnp.arange(EXPERTS, dtype=jnp.int32)[None, :]).astype(jnp.int32), axis=0)
    offsets = (jnp.cumsum(counts) - counts).astype(jnp.int32)
    padded = jnp.concatenate([order, jnp.zeros((span,), jnp.int32)])
    hidden_local = HID // N_BLK
    contract_cols = (((1,), (1,)), ((), ()))
    contract_rows = (((0,), (0,)), ((), ()))

    def one_expert(expert):
        picks = lax.dynamic_slice_in_dim(padded, offsets[expert].astype(jnp.int32), span)
        valid = jnp.arange(span, dtype=jnp.int32) < counts[expert]
        rows_tok = (picks // TOPK).astype(jnp.int32)
        rows_pick = (picks % TOPK).astype(jnp.int32)
        feats = jnp.where(valid[:, None], tokens[rows_tok], jnp.zeros_like(tokens[rows_tok]))
        cotan = jnp.where(valid[:, None], grad_out[rows_tok], jnp.zeros_like(grad_out[rows_tok]))
        gates = jnp.where(valid, gate_weights[rows_tok, rows_pick].astype(jnp.float32), jnp.float32(0.0))
        wgate = dequantize(gate_codes[expert], block_scales[expert, 0])
        wup = dequantize(up_codes[expert], block_scales[expert, 1])
        wdown = dequantize(down_codes[expert], block_scales[expert, 2])
        gate_pre = jnp.dot(feats, wgate, preferred_element_type=jnp.float32)
        up_pre = jnp.dot(feats, wup, preferred_element_type=jnp.float32)
        down_back = jnp.dot(cotan, wdown, preferred_element_type=jnp.float32)
        hidden, grad_gate, grad_up, gated_hidden = backward_math(gate_pre, up_pre, down_back, gates)
        contrib = jnp.zeros((span, width), jnp.float32)
        gate_sum = jnp.zeros((span,), jnp.float32)
        for number in range(N_BLK):
            lower = number * hidden_local
            upper = lower + hidden_local
            partial_value = lax.dot_general(grad_gate[:, lower:upper], wgate[:, lower:upper], contract_cols, preferred_element_type=jnp.float32)
            partial_value = partial_value + lax.dot_general(grad_up[:, lower:upper], wup[:, lower:upper], contract_cols, preferred_element_type=jnp.float32)
            contrib = contrib + lax.optimization_barrier(partial_value.astype(jnp.bfloat16)).astype(jnp.float32)
            scores = jnp.sum(hidden[:, lower:upper] * down_back[:, lower:upper], axis=1)
            gate_sum = gate_sum + lax.optimization_barrier(scores.astype(jnp.bfloat16)).astype(jnp.float32)
        gate_grad = lax.dot_general(feats, grad_gate, contract_rows, preferred_element_type=jnp.float32).astype(jnp.bfloat16)
        up_grad = lax.dot_general(feats, grad_up, contract_rows, preferred_element_type=jnp.float32).astype(jnp.bfloat16)
        down_grad = lax.dot_general(cotan, gated_hidden, contract_rows, preferred_element_type=jnp.float32).astype(jnp.bfloat16)
        return contrib.astype(jnp.bfloat16), gate_sum.astype(jnp.bfloat16), gate_grad, up_grad, down_grad, rows_tok, rows_pick, valid

    results = lax.map(one_expert, jnp.arange(EXPERTS, dtype=jnp.int32))
    contrib, gate_sum, gate_grad, up_grad, down_grad, rows_tok, rows_pick, valid = results
    contrib_f = jnp.where(valid[:, :, None], contrib.astype(jnp.float32), jnp.float32(0.0))
    grad_tokens = jnp.zeros((tokens.shape[0], width), jnp.float32)
    grad_tokens = grad_tokens.at[rows_tok.reshape(-1)].add(contrib_f.reshape(-1, width))
    gate_f = jnp.where(valid, gate_sum.astype(jnp.float32), jnp.float32(0.0))
    grad_gates = jnp.zeros((tokens.shape[0], TOPK), jnp.float32)
    grad_gates = grad_gates.at[rows_tok.reshape(-1), rows_pick.reshape(-1)].add(gate_f.reshape(-1))
    return (grad_tokens.astype(jnp.bfloat16), grad_gates.astype(jnp.bfloat16), gate_grad, up_grad, down_grad)
```

```python
import jax
import jax.numpy as jnp
from jax import lax
from jax.sharding import PartitionSpec as P

QBLOCK = 128
TOPK = 2
LANE = 128


def dequantize(codes, scales):
    rows_in, cols_in = codes.shape
    blocks = codes.astype(jnp.float32).reshape(rows_in // QBLOCK, QBLOCK, cols_in // QBLOCK, QBLOCK)
    scaled = blocks * jnp.transpose(scales.astype(jnp.float32))[:, None, :, None]
    return scaled.reshape(rows_in, cols_in).astype(jnp.bfloat16)


def backward_math(gate_pre, up_pre, down_back, gates):
    sigma = jax.nn.sigmoid(gate_pre)
    hidden = gate_pre * sigma * up_pre
    grad_hidden = gates[:, None] * down_back
    grad_up = (grad_hidden * gate_pre * sigma).astype(jnp.bfloat16)
    grad_gate = (grad_hidden * up_pre * sigma * (1.0 + gate_pre * (1.0 - sigma))).astype(
        jnp.bfloat16
    )
    gated_hidden = (gates[:, None] * hidden).astype(jnp.bfloat16)
    return (hidden, grad_gate, grad_up, gated_hidden)


def routing_tables(expert_ids, experts, capacity):
    route_hot = (
        expert_ids[:, :, None] == jnp.arange(experts, dtype=jnp.int32)[None, None, :]
    ).astype(jnp.int32)
    chosen = jnp.sum(route_hot, axis=1)
    earlier = jnp.cumsum(chosen, axis=0) - chosen
    slot_hot = (earlier[:, :, None] == jnp.arange(capacity, dtype=jnp.int32)[None, None, :]).astype(
        jnp.int32
    )
    placed = chosen[:, :, None] * slot_hot
    picked = route_hot[:, :, :, None] * slot_hot[:, None, :, :]
    return (placed.astype(jnp.float32), picked.astype(jnp.float32))


def project_back(grad_gate, grad_up, wgate, wup):
    contract_cols = (((1,), (1,)), ((), ()))
    partial_value = lax.dot_general(
        grad_gate, wgate, contract_cols, preferred_element_type=jnp.float32
    )
    return partial_value + lax.dot_general(
        grad_up, wup, contract_cols, preferred_element_type=jnp.float32
    )


def row_sum(left, right):
    return lax.dot_general(
        left, right, (((0,), (0,)), ((), ())), preferred_element_type=jnp.float32
    )


def on_device(
    tokens, grad_out, expert_ids, gate_weights, gate_codes, up_codes, down_codes, block_scales
):
    experts = lax.axis_size("eg")
    width = tokens.shape[1]
    capacity = 2 * tokens.shape[0] * TOPK // experts
    placed, picked = routing_tables(expert_ids, experts, capacity)
    placed_low = placed.astype(jnp.bfloat16)
    both = jnp.concatenate([tokens, grad_out], axis=1)
    send_rows = jnp.einsum(
        "tec,td->ecd", placed_low, both, preferred_element_type=jnp.float32
    ).astype(jnp.bfloat16)
    send_gates = jnp.einsum(
        "tkec,tk->ec", picked, gate_weights.astype(jnp.float32), precision=lax.Precision.HIGHEST
    ).astype(jnp.bfloat16)
    gate_block = jnp.pad(send_gates[:, :, None], ((0, 0), (0, 0), (0, LANE - 1)))
    send = jnp.concatenate([send_rows, gate_block], axis=2)
    recv = lax.all_to_all(send, "eg", split_axis=0, concat_axis=0, tiled=True)
    recv = recv.reshape(experts * capacity, recv.shape[2])
    wgate = dequantize(gate_codes[0], block_scales[0, 0])
    wup = dequantize(up_codes[0], block_scales[0, 1])
    wdown = dequantize(down_codes[0], block_scales[0, 2])
    gathered = lax.all_gather(recv, "blk", axis=0, tiled=True)
    feats = gathered[:, :width]
    cotan = gathered[:, width : 2 * width]
    gates = gathered[:, 2 * width].astype(jnp.float32)
    gate_pre = jnp.dot(feats, wgate, preferred_element_type=jnp.float32)
    up_pre = jnp.dot(feats, wup, preferred_element_type=jnp.float32)
    down_back = jnp.dot(cotan, wdown, preferred_element_type=jnp.float32)
    hidden, grad_gate, grad_up, gated_hidden = backward_math(gate_pre, up_pre, down_back, gates)
    contrib = project_back(grad_gate, grad_up, wgate, wup).astype(jnp.bfloat16)
    scores = jnp.sum(hidden * down_back, axis=1).astype(jnp.bfloat16)
    score_block = jnp.pad(scores[:, None], ((0, 0), (0, LANE - 1)))
    partial_rows = jnp.concatenate([contrib, score_block], axis=1)
    summed = lax.psum_scatter(partial_rows, "blk", scatter_dimension=0, tiled=True)
    gate_grad = row_sum(feats, grad_gate).astype(jnp.bfloat16)[None]
    up_grad = row_sum(feats, grad_up).astype(jnp.bfloat16)[None]
    down_grad = row_sum(cotan, gated_hidden).astype(jnp.bfloat16)[None]
    summed = summed.reshape(experts, capacity, summed.shape[1])
    home = lax.all_to_all(summed, "eg", split_axis=0, concat_axis=0, tiled=True)
    grad_tokens = jnp.einsum(
        "tec,ecd->td", placed_low, home[:, :, :width], preferred_element_type=jnp.float32
    ).astype(jnp.bfloat16)
    grad_gates = jnp.einsum(
        "tkec,ec->tk",
        picked,
        home[:, :, width].astype(jnp.float32),
        precision=lax.Precision.HIGHEST,
    ).astype(jnp.bfloat16)
    return (grad_tokens, grad_gates, gate_grad, up_grad, down_grad)


def solution(mesh):
    in_specs = (
        P(("eg", "blk"), None),
        P(("eg", "blk"), None),
        P(("eg", "blk"), None),
        P(("eg", "blk"), None),
        P("eg", None, "blk"),
        P("eg", None, "blk"),
        P("eg", None, "blk"),
        P("eg", None, "blk", None),
    )
    out_specs = (
        P(("eg", "blk"), None),
        P(("eg", "blk"), None),
        P("eg", None, "blk"),
        P("eg", None, "blk"),
        P("eg", None, "blk"),
    )
    return jax.shard_map(
        on_device, mesh=mesh, in_specs=in_specs, out_specs=out_specs, check_vma=False
    )
```

```python
import jax
import jax.numpy as jnp
from jax import lax
from jax.sharding import PartitionSpec as P

QBLOCK = 128
TOPK = 2
LANE = 128


def dequantize(codes, scales):
    rows_in, cols_in = codes.shape
    blocks = codes.astype(jnp.float32).reshape(rows_in // QBLOCK, QBLOCK, cols_in // QBLOCK, QBLOCK)
    scaled = blocks * jnp.transpose(scales.astype(jnp.float32))[:, None, :, None]
    return scaled.reshape(rows_in, cols_in).astype(jnp.bfloat16)


def backward_math(gate_pre, up_pre, down_back, gates):
    sigma = jax.nn.sigmoid(gate_pre)
    hidden = gate_pre * sigma * up_pre
    grad_hidden = gates[:, None] * down_back
    grad_up = (grad_hidden * gate_pre * sigma).astype(jnp.bfloat16)
    grad_gate = (grad_hidden * up_pre * sigma * (1.0 + gate_pre * (1.0 - sigma))).astype(
        jnp.bfloat16
    )
    gated_hidden = (gates[:, None] * hidden).astype(jnp.bfloat16)
    return (hidden, grad_gate, grad_up, gated_hidden)


def routing_tables(expert_ids, experts, capacity):
    route_hot = (
        expert_ids[:, :, None] == jnp.arange(experts, dtype=jnp.int32)[None, None, :]
    ).astype(jnp.int32)
    chosen = jnp.sum(route_hot, axis=1)
    earlier = jnp.cumsum(chosen, axis=0) - chosen
    slot_hot = (earlier[:, :, None] == jnp.arange(capacity, dtype=jnp.int32)[None, None, :]).astype(
        jnp.int32
    )
    placed = chosen[:, :, None] * slot_hot
    picked = route_hot[:, :, :, None] * slot_hot[:, None, :, :]
    return (placed.astype(jnp.float32), picked.astype(jnp.float32))


def project_back(grad_gate, grad_up, wgate, wup):
    contract_cols = (((1,), (1,)), ((), ()))
    partial_value = lax.dot_general(
        grad_gate, wgate, contract_cols, preferred_element_type=jnp.float32
    )
    return partial_value + lax.dot_general(
        grad_up, wup, contract_cols, preferred_element_type=jnp.float32
    )


def row_sum(left, right):
    return lax.dot_general(
        left, right, (((0,), (0,)), ((), ())), preferred_element_type=jnp.float32
    )


def on_device(
    tokens, grad_out, expert_ids, gate_weights, gate_codes, up_codes, down_codes, block_scales
):
    experts = lax.axis_size("eg")
    width = tokens.shape[1]
    capacity = 2 * tokens.shape[0] * TOPK // experts
    placed, picked = routing_tables(expert_ids, experts, capacity)
    placed_low = placed.astype(jnp.bfloat16)
    both = jnp.concatenate([tokens, grad_out], axis=1)
    send_rows = jnp.einsum(
        "tec,td->ecd", placed_low, both, preferred_element_type=jnp.float32
    ).astype(jnp.bfloat16)
    send_gates = jnp.einsum(
        "tkec,tk->ec", picked, gate_weights.astype(jnp.float32), precision=lax.Precision.HIGHEST
    ).astype(jnp.bfloat16)
    gate_block = jnp.pad(send_gates[:, :, None], ((0, 0), (0, 0), (0, LANE - 1)))
    send = jnp.concatenate([send_rows, gate_block], axis=2)
    recv = lax.all_to_all(send, "eg", split_axis=0, concat_axis=0, tiled=True)
    wgate = dequantize(gate_codes[0], block_scales[0, 0])
    wup = dequantize(up_codes[0], block_scales[0, 1])
    wdown = dequantize(down_codes[0], block_scales[0, 2])
    summed_slots = []
    grads = None
    for slot in range(capacity):
        gathered = lax.all_gather(recv[:, slot, :], "blk", axis=0, tiled=True)
        feats = gathered[:, :width]
        cotan = gathered[:, width : 2 * width]
        gates = gathered[:, 2 * width].astype(jnp.float32)
        gate_pre = jnp.dot(feats, wgate, preferred_element_type=jnp.float32)
        up_pre = jnp.dot(feats, wup, preferred_element_type=jnp.float32)
        down_back = jnp.dot(cotan, wdown, preferred_element_type=jnp.float32)
        hidden, grad_gate, grad_up, gated_hidden = backward_math(
            gate_pre, up_pre, down_back, gates
        )
        contrib = project_back(grad_gate, grad_up, wgate, wup).astype(jnp.bfloat16)
        scores = jnp.sum(hidden * down_back, axis=1).astype(jnp.bfloat16)
        score_block = jnp.pad(scores[:, None], ((0, 0), (0, LANE - 1)))
        partial_rows = jnp.concatenate([contrib, score_block], axis=1)
        summed_slots.append(lax.psum_scatter(partial_rows, "blk", scatter_dimension=0, tiled=True))
        chunk = (
            row_sum(feats, grad_gate),
            row_sum(feats, grad_up),
            row_sum(cotan, gated_hidden),
        )
        grads = chunk if grads is None else tuple(a + b for a, b in zip(grads, chunk))
    gate_grad, up_grad, down_grad = (g.astype(jnp.bfloat16)[None] for g in grads)
    summed = jnp.stack(summed_slots, axis=1)
    home = lax.all_to_all(summed, "eg", split_axis=0, concat_axis=0, tiled=True)
    grad_tokens = jnp.einsum(
        "tec,ecd->td", placed_low, home[:, :, :width], preferred_element_type=jnp.float32
    ).astype(jnp.bfloat16)
    grad_gates = jnp.einsum(
        "tkec,ec->tk",
        picked,
        home[:, :, width].astype(jnp.float32),
        precision=lax.Precision.HIGHEST,
    ).astype(jnp.bfloat16)
    return (grad_tokens, grad_gates, gate_grad, up_grad, down_grad)


def solution(mesh):
    in_specs = (
        P(("eg", "blk"), None),
        P(("eg", "blk"), None),
        P(("eg", "blk"), None),
        P(("eg", "blk"), None),
        P("eg", None, "blk"),
        P("eg", None, "blk"),
        P("eg", None, "blk"),
        P("eg", None, "blk", None),
    )
    out_specs = (
        P(("eg", "blk"), None),
        P(("eg", "blk"), None),
        P("eg", None, "blk"),
        P("eg", None, "blk"),
        P("eg", None, "blk"),
    )
    return jax.shard_map(
        on_device, mesh=mesh, in_specs=in_specs, out_specs=out_specs, check_vma=False
    )
```

```python
import jax
import jax.numpy as jnp
from jax import lax
from jax.sharding import PartitionSpec as P

QBLOCK = 128
TOPK = 2
LANE = 128


def dequantize(codes, scales):
    rows_in, cols_in = codes.shape
    blocks = codes.astype(jnp.float32).reshape(rows_in // QBLOCK, QBLOCK, cols_in // QBLOCK, QBLOCK)
    scaled = blocks * jnp.transpose(scales.astype(jnp.float32))[:, None, :, None]
    return scaled.reshape(rows_in, cols_in).astype(jnp.bfloat16)


def backward_math(gate_pre, up_pre, down_back, gates):
    sigma = jax.nn.sigmoid(gate_pre)
    hidden = gate_pre * sigma * up_pre
    grad_hidden = gates[:, None] * down_back
    grad_up = (grad_hidden * gate_pre * sigma).astype(jnp.bfloat16)
    grad_gate = (grad_hidden * up_pre * sigma * (1.0 + gate_pre * (1.0 - sigma))).astype(
        jnp.bfloat16
    )
    gated_hidden = (gates[:, None] * hidden).astype(jnp.bfloat16)
    return (hidden, grad_gate, grad_up, gated_hidden)


def routing_tables(expert_ids, experts, capacity):
    route_hot = (
        expert_ids[:, :, None] == jnp.arange(experts, dtype=jnp.int32)[None, None, :]
    ).astype(jnp.int32)
    chosen = jnp.sum(route_hot, axis=1)
    earlier = jnp.cumsum(chosen, axis=0) - chosen
    slot_hot = (earlier[:, :, None] == jnp.arange(capacity, dtype=jnp.int32)[None, None, :]).astype(
        jnp.int32
    )
    placed = chosen[:, :, None] * slot_hot
    picked = route_hot[:, :, :, None] * slot_hot[:, None, :, :]
    return (placed.astype(jnp.float32), picked.astype(jnp.float32))


def project_back(grad_gate, grad_up, wgate, wup):
    contract_cols = (((1,), (1,)), ((), ()))
    partial_value = lax.dot_general(
        grad_gate, wgate, contract_cols, preferred_element_type=jnp.float32
    )
    return partial_value + lax.dot_general(
        grad_up, wup, contract_cols, preferred_element_type=jnp.float32
    )


def row_sum(left, right):
    return lax.dot_general(
        left, right, (((0,), (0,)), ((), ())), preferred_element_type=jnp.float32
    )


def on_device(
    tokens, grad_out, expert_ids, gate_weights, gate_codes, up_codes, down_codes, block_scales
):
    experts = lax.axis_size("eg")
    width = tokens.shape[1]
    capacity = 2 * tokens.shape[0] * TOPK // experts
    placed, picked = routing_tables(expert_ids, experts, capacity)
    placed_low = placed.astype(jnp.bfloat16)
    both = jnp.concatenate([tokens, grad_out], axis=1)
    send_rows = jnp.einsum(
        "tec,td->ecd", placed_low, both, preferred_element_type=jnp.float32
    ).astype(jnp.bfloat16)
    send_gates = jnp.einsum(
        "tkec,tk->ec", picked, gate_weights.astype(jnp.float32), precision=lax.Precision.HIGHEST
    ).astype(jnp.bfloat16)
    gate_block = jnp.pad(send_gates[:, :, None], ((0, 0), (0, 0), (0, LANE - 1)))
    send = jnp.concatenate([send_rows, gate_block], axis=2)
    recv = lax.all_to_all(send, "eg", split_axis=0, concat_axis=0, tiled=True)
    recv = recv.reshape(experts * capacity, recv.shape[2])
    wgate = dequantize(gate_codes[0], block_scales[0, 0])
    wup = dequantize(up_codes[0], block_scales[0, 1])
    wdown = dequantize(down_codes[0], block_scales[0, 2])
    hid = wgate.shape[1]
    wboth = jnp.concatenate([wgate, wup], axis=1)
    wboth_ext = jnp.pad(wboth, ((0, LANE), (0, 0)))
    gathered = lax.all_gather(recv, "blk", axis=0, tiled=True)
    feats = gathered[:, :width]
    cotan = gathered[:, width : 2 * width]
    gates = gathered[:, 2 * width].astype(jnp.float32)
    both_pre = jnp.dot(feats, wboth, preferred_element_type=jnp.float32)
    gate_pre = both_pre[:, :hid]
    up_pre = both_pre[:, hid:]
    down_back = jnp.dot(cotan, wdown, preferred_element_type=jnp.float32)
    hidden, grad_gate, grad_up, gated_hidden = backward_math(gate_pre, up_pre, down_back, gates)
    grad_both = jnp.concatenate([grad_gate, grad_up], axis=1)
    back = lax.dot_general(
        grad_both, wboth_ext, (((1,), (1,)), ((), ())), preferred_element_type=jnp.float32
    )
    scores = jnp.sum(hidden * down_back, axis=1).astype(jnp.bfloat16).astype(jnp.float32)
    column = lax.broadcasted_iota(jnp.int32, back.shape, 1)
    partial_rows = jnp.where(column == width, scores[:, None], back).astype(jnp.bfloat16)
    summed = lax.psum_scatter(partial_rows, "blk", scatter_dimension=0, tiled=True)
    both_grad = row_sum(feats, grad_both).astype(jnp.bfloat16)
    gate_grad = both_grad[None, :, :hid]
    up_grad = both_grad[None, :, hid:]
    down_grad = row_sum(cotan, gated_hidden).astype(jnp.bfloat16)[None]
    summed, gate_grad, up_grad, down_grad = lax.optimization_barrier(
        (summed, gate_grad, up_grad, down_grad)
    )
    summed = summed.reshape(experts, capacity, summed.shape[1])
    home = lax.all_to_all(summed, "eg", split_axis=0, concat_axis=0, tiled=True)
    grad_tokens = jnp.einsum(
        "tec,ecd->td", placed_low, home[:, :, :width], preferred_element_type=jnp.float32
    ).astype(jnp.bfloat16)
    grad_gates = jnp.einsum(
        "tkec,ec->tk",
        picked,
        home[:, :, width].astype(jnp.float32),
        precision=lax.Precision.HIGHEST,
    ).astype(jnp.bfloat16)
    return (grad_tokens, grad_gates, gate_grad, up_grad, down_grad)


def solution(mesh):
    in_specs = (
        P(("eg", "blk"), None),
        P(("eg", "blk"), None),
        P(("eg", "blk"), None),
        P(("eg", "blk"), None),
        P("eg", None, "blk"),
        P("eg", None, "blk"),
        P("eg", None, "blk"),
        P("eg", None, "blk", None),
    )
    out_specs = (
        P(("eg", "blk"), None),
        P(("eg", "blk"), None),
        P("eg", None, "blk"),
        P("eg", None, "blk"),
        P("eg", None, "blk"),
    )
    return jax.shard_map(
        on_device, mesh=mesh, in_specs=in_specs, out_specs=out_specs, check_vma=False
    )
```

```python
import jax
import jax.numpy as jnp
from jax import lax
from jax.sharding import PartitionSpec as P

QBLOCK = 128
TOPK = 2
LANE = 128


def dequantize(codes, scales):
    rows_in, cols_in = codes.shape
    blocks = codes.astype(jnp.float32).reshape(rows_in // QBLOCK, QBLOCK, cols_in // QBLOCK, QBLOCK)
    scaled = blocks * jnp.transpose(scales.astype(jnp.float32))[:, None, :, None]
    return scaled.reshape(rows_in, cols_in).astype(jnp.bfloat16)


def backward_math(gate_pre, up_pre, down_back, gates):
    sigma = jax.nn.sigmoid(gate_pre)
    hidden = gate_pre * sigma * up_pre
    grad_hidden = gates[:, None] * down_back
    grad_up = (grad_hidden * gate_pre * sigma).astype(jnp.bfloat16)
    grad_gate = (grad_hidden * up_pre * sigma * (1.0 + gate_pre * (1.0 - sigma))).astype(
        jnp.bfloat16
    )
    gated_hidden = (gates[:, None] * hidden).astype(jnp.bfloat16)
    return (hidden, grad_gate, grad_up, gated_hidden)


def routing_tables(expert_ids, experts, capacity):
    route_hot = (
        expert_ids[:, :, None] == jnp.arange(experts, dtype=jnp.int32)[None, None, :]
    ).astype(jnp.int32)
    chosen = jnp.sum(route_hot, axis=1)
    earlier = jnp.cumsum(chosen, axis=0) - chosen
    slot_hot = (earlier[:, :, None] == jnp.arange(capacity, dtype=jnp.int32)[None, None, :]).astype(
        jnp.int32
    )
    placed = chosen[:, :, None] * slot_hot
    picked = route_hot[:, :, :, None] * slot_hot[:, None, :, :]
    return (placed.astype(jnp.float32), picked.astype(jnp.float32))


def project_back(grad_gate, grad_up, wgate, wup):
    contract_cols = (((1,), (1,)), ((), ()))
    partial_value = lax.dot_general(
        grad_gate, wgate, contract_cols, preferred_element_type=jnp.float32
    )
    return partial_value + lax.dot_general(
        grad_up, wup, contract_cols, preferred_element_type=jnp.float32
    )


def row_sum(left, right):
    return lax.dot_general(
        left, right, (((0,), (0,)), ((), ())), preferred_element_type=jnp.float32
    )


def shift_exchange(blocks, count, sign):
    moved = [blocks[0]]
    for k in range(1, count):
        perm = [(j, (j + sign * k) % count) for j in range(count)]
        moved.append(lax.ppermute(blocks[k], "eg", perm))
    return jnp.stack(moved, axis=0)


def on_device(
    tokens, grad_out, expert_ids, gate_weights, gate_codes, up_codes, down_codes, block_scales
):
    experts = lax.axis_size("eg")
    width = tokens.shape[1]
    capacity = 2 * tokens.shape[0] * TOPK // experts
    own = lax.axis_index("eg")
    relative_ids = (expert_ids - own) % experts
    placed, picked = routing_tables(relative_ids, experts, capacity)
    placed_low = placed.astype(jnp.bfloat16)
    both = jnp.concatenate([tokens, grad_out], axis=1)
    send_rows = jnp.einsum(
        "tec,td->ecd", placed_low, both, preferred_element_type=jnp.float32
    ).astype(jnp.bfloat16)
    send_gates = jnp.einsum(
        "tkec,tk->ec", picked, gate_weights.astype(jnp.float32), precision=lax.Precision.HIGHEST
    ).astype(jnp.bfloat16)
    gate_block = jnp.pad(send_gates[:, :, None], ((0, 0), (0, 0), (0, LANE - 1)))
    send = jnp.concatenate([send_rows, gate_block], axis=2)
    recv = shift_exchange(send, experts, 1)
    recv = recv.reshape(experts * capacity, recv.shape[2])
    wgate = dequantize(gate_codes[0], block_scales[0, 0])
    wup = dequantize(up_codes[0], block_scales[0, 1])
    wdown = dequantize(down_codes[0], block_scales[0, 2])
    hid = wgate.shape[1]
    wboth = jnp.concatenate([wgate, wup], axis=1)
    wboth_ext = jnp.pad(wboth, ((0, LANE), (0, 0)))
    gathered = lax.all_gather(recv, "blk", axis=0, tiled=True)
    feats = gathered[:, :width]
    cotan = gathered[:, width : 2 * width]
    gates = gathered[:, 2 * width].astype(jnp.float32)
    both_pre = jnp.dot(feats, wboth, preferred_element_type=jnp.float32)
    gate_pre = both_pre[:, :hid]
    up_pre = both_pre[:, hid:]
    down_back = jnp.dot(cotan, wdown, preferred_element_type=jnp.float32)
    hidden, grad_gate, grad_up, gated_hidden = backward_math(gate_pre, up_pre, down_back, gates)
    grad_both = jnp.concatenate([grad_gate, grad_up], axis=1)
    back = lax.dot_general(
        grad_both, wboth_ext, (((1,), (1,)), ((), ())), preferred_element_type=jnp.float32
    )
    scores = jnp.sum(hidden * down_back, axis=1).astype(jnp.bfloat16).astype(jnp.float32)
    column = lax.broadcasted_iota(jnp.int32, back.shape, 1)
    partial_rows = jnp.where(column == width, scores[:, None], back).astype(jnp.bfloat16)
    summed = lax.psum_scatter(partial_rows, "blk", scatter_dimension=0, tiled=True)
    both_grad = row_sum(feats, grad_both).astype(jnp.bfloat16)
    gate_grad = both_grad[None, :, :hid]
    up_grad = both_grad[None, :, hid:]
    down_grad = row_sum(cotan, gated_hidden).astype(jnp.bfloat16)[None]
    summed, gate_grad, up_grad, down_grad = lax.optimization_barrier(
        (summed, gate_grad, up_grad, down_grad)
    )
    summed = summed.reshape(experts, capacity, summed.shape[1])
    home = shift_exchange(summed, experts, -1)
    grad_tokens = jnp.einsum(
        "tec,ecd->td", placed_low, home[:, :, :width], preferred_element_type=jnp.float32
    ).astype(jnp.bfloat16)
    grad_gates = jnp.einsum(
        "tkec,ec->tk",
        picked,
        home[:, :, width].astype(jnp.float32),
        precision=lax.Precision.HIGHEST,
    ).astype(jnp.bfloat16)
    return (grad_tokens, grad_gates, gate_grad, up_grad, down_grad)


def solution(mesh):
    in_specs = (
        P(("eg", "blk"), None),
        P(("eg", "blk"), None),
        P(("eg", "blk"), None),
        P(("eg", "blk"), None),
        P("eg", None, "blk"),
        P("eg", None, "blk"),
        P("eg", None, "blk"),
        P("eg", None, "blk", None),
    )
    out_specs = (
        P(("eg", "blk"), None),
        P(("eg", "blk"), None),
        P("eg", None, "blk"),
        P("eg", None, "blk"),
        P("eg", None, "blk"),
    )
    return jax.shard_map(
        on_device, mesh=mesh, in_specs=in_specs, out_specs=out_specs, check_vma=False
    )
```

```python
import jax
import jax.numpy as jnp
from jax import lax
from jax.sharding import Mesh
from jax.sharding import PartitionSpec as P

QBLOCK = 128
TOPK = 2
LANE = 128


def dequantize(codes, scales):
    rows_in, cols_in = codes.shape
    blocks = codes.astype(jnp.float32).reshape(rows_in // QBLOCK, QBLOCK, cols_in // QBLOCK, QBLOCK)
    scaled = blocks * jnp.transpose(scales.astype(jnp.float32))[:, None, :, None]
    return scaled.reshape(rows_in, cols_in).astype(jnp.bfloat16)


def backward_math(gate_pre, up_pre, down_back, gates):
    sigma = jax.nn.sigmoid(gate_pre)
    hidden = gate_pre * sigma * up_pre
    grad_hidden = gates[:, None] * down_back
    grad_up = (grad_hidden * gate_pre * sigma).astype(jnp.bfloat16)
    grad_gate = (grad_hidden * up_pre * sigma * (1.0 + gate_pre * (1.0 - sigma))).astype(
        jnp.bfloat16
    )
    gated_hidden = (gates[:, None] * hidden).astype(jnp.bfloat16)
    return (hidden, grad_gate, grad_up, gated_hidden)


def routing_tables(expert_ids, experts, capacity):
    route_hot = (
        expert_ids[:, :, None] == jnp.arange(experts, dtype=jnp.int32)[None, None, :]
    ).astype(jnp.int32)
    chosen = jnp.sum(route_hot, axis=1)
    earlier = jnp.cumsum(chosen, axis=0) - chosen
    slot_hot = (earlier[:, :, None] == jnp.arange(capacity, dtype=jnp.int32)[None, None, :]).astype(
        jnp.int32
    )
    placed = chosen[:, :, None] * slot_hot
    picked = route_hot[:, :, :, None] * slot_hot[:, None, :, :]
    return (placed.astype(jnp.float32), picked.astype(jnp.float32))


def project_back(grad_gate, grad_up, wgate, wup):
    contract_cols = (((1,), (1,)), ((), ()))
    partial_value = lax.dot_general(
        grad_gate, wgate, contract_cols, preferred_element_type=jnp.float32
    )
    return partial_value + lax.dot_general(
        grad_up, wup, contract_cols, preferred_element_type=jnp.float32
    )


def row_sum(left, right):
    return lax.dot_general(
        left, right, (((0,), (0,)), ((), ())), preferred_element_type=jnp.float32
    )


def on_device(
    tokens, grad_out, expert_ids, gate_weights, gate_codes, up_codes, down_codes, block_scales
):
    experts = lax.axis_size("eg")
    width = tokens.shape[1]
    capacity = 2 * tokens.shape[0] * TOPK // experts
    placed, picked = routing_tables(expert_ids, experts, capacity)
    placed_low = placed.astype(jnp.bfloat16)
    both = jnp.concatenate([tokens, grad_out], axis=1)
    send_rows = jnp.einsum(
        "tec,td->ecd", placed_low, both, preferred_element_type=jnp.float32
    ).astype(jnp.bfloat16)
    send_gates = jnp.einsum(
        "tkec,tk->ec", picked, gate_weights.astype(jnp.float32), precision=lax.Precision.HIGHEST
    ).astype(jnp.bfloat16)
    gate_block = jnp.pad(send_gates[:, :, None], ((0, 0), (0, 0), (0, LANE - 1)))
    send = jnp.concatenate([send_rows, gate_block], axis=2)
    recv = lax.all_to_all(send, "eg", split_axis=0, concat_axis=0, tiled=True)
    recv = recv.reshape(experts * capacity, recv.shape[2])
    wgate = dequantize(gate_codes[0], block_scales[0, 0])
    wup = dequantize(up_codes[0], block_scales[0, 1])
    wdown = dequantize(down_codes[0], block_scales[0, 2])
    hid = wgate.shape[1]
    wboth = jnp.concatenate([wgate, wup], axis=1)
    wboth_ext = jnp.pad(wboth, ((0, LANE), (0, 0)))
    gathered = lax.all_gather(recv, "chip", axis=0, tiled=True)
    gathered = lax.all_gather(gathered, "core", axis=0, tiled=True)
    feats = gathered[:, :width]
    cotan = gathered[:, width : 2 * width]
    gates = gathered[:, 2 * width].astype(jnp.float32)
    both_pre = jnp.dot(feats, wboth, preferred_element_type=jnp.float32)
    gate_pre = both_pre[:, :hid]
    up_pre = both_pre[:, hid:]
    down_back = jnp.dot(cotan, wdown, preferred_element_type=jnp.float32)
    hidden, grad_gate, grad_up, gated_hidden = backward_math(gate_pre, up_pre, down_back, gates)
    grad_both = jnp.concatenate([grad_gate, grad_up], axis=1)
    back = lax.dot_general(
        grad_both, wboth_ext, (((1,), (1,)), ((), ())), preferred_element_type=jnp.float32
    )
    scores = jnp.sum(hidden * down_back, axis=1).astype(jnp.bfloat16).astype(jnp.float32)
    column = lax.broadcasted_iota(jnp.int32, back.shape, 1)
    partial_rows = jnp.where(column == width, scores[:, None], back).astype(jnp.bfloat16)
    summed = lax.psum_scatter(partial_rows, "core", scatter_dimension=0, tiled=True)
    summed = lax.psum_scatter(summed, "chip", scatter_dimension=0, tiled=True)
    both_grad = row_sum(feats, grad_both).astype(jnp.bfloat16)
    gate_grad = both_grad[None, :, :hid]
    up_grad = both_grad[None, :, hid:]
    down_grad = row_sum(cotan, gated_hidden).astype(jnp.bfloat16)[None]
    summed, gate_grad, up_grad, down_grad = lax.optimization_barrier(
        (summed, gate_grad, up_grad, down_grad)
    )
    summed = summed.reshape(experts, capacity, summed.shape[1])
    home = lax.all_to_all(summed, "eg", split_axis=0, concat_axis=0, tiled=True)
    grad_tokens = jnp.einsum(
        "tec,ecd->td", placed_low, home[:, :, :width], preferred_element_type=jnp.float32
    ).astype(jnp.bfloat16)
    grad_gates = jnp.einsum(
        "tkec,ec->tk",
        picked,
        home[:, :, width].astype(jnp.float32),
        precision=lax.Precision.HIGHEST,
    ).astype(jnp.bfloat16)
    return (grad_tokens, grad_gates, gate_grad, up_grad, down_grad)


def solution(mesh):
    n_eg, n_blk = mesh.devices.shape
    split = Mesh(mesh.devices.reshape(n_eg, n_blk // 2, 2), ("eg", "chip", "core"))
    blk = ("chip", "core")
    in_specs = (
        P(("eg",) + blk, None),
        P(("eg",) + blk, None),
        P(("eg",) + blk, None),
        P(("eg",) + blk, None),
        P("eg", None, blk),
        P("eg", None, blk),
        P("eg", None, blk),
        P("eg", None, blk, None),
    )
    out_specs = (
        P(("eg",) + blk, None),
        P(("eg",) + blk, None),
        P("eg", None, blk),
        P("eg", None, blk),
        P("eg", None, blk),
    )
    return jax.shard_map(
        on_device, mesh=split, in_specs=in_specs, out_specs=out_specs, check_vma=False
    )
```

```python
import jax
import jax.numpy as jnp
from jax import lax
from jax.sharding import Mesh
from jax.sharding import PartitionSpec as P

QBLOCK = 128
TOPK = 2
LANE = 128
BLK = ("chip", "core")


def dequantize(codes, scales):
    rows_in, cols_in = codes.shape
    blocks = codes.astype(jnp.float32).reshape(rows_in // QBLOCK, QBLOCK, cols_in // QBLOCK, QBLOCK)
    scaled = blocks * jnp.transpose(scales.astype(jnp.float32))[:, None, :, None]
    return scaled.reshape(rows_in, cols_in).astype(jnp.bfloat16)


def backward_math(gate_pre, up_pre, down_back, gates):
    sigma = jax.nn.sigmoid(gate_pre)
    hidden = gate_pre * sigma * up_pre
    grad_hidden = gates[:, None] * down_back
    grad_up = (grad_hidden * gate_pre * sigma).astype(jnp.bfloat16)
    grad_gate = (grad_hidden * up_pre * sigma * (1.0 + gate_pre * (1.0 - sigma))).astype(
        jnp.bfloat16
    )
    gated_hidden = (gates[:, None] * hidden).astype(jnp.bfloat16)
    return (hidden, grad_gate, grad_up, gated_hidden)


def routing_tables(expert_ids, experts, capacity):
    route_hot = (
        expert_ids[:, :, None] == jnp.arange(experts, dtype=jnp.int32)[None, None, :]
    ).astype(jnp.int32)
    chosen = jnp.sum(route_hot, axis=1)
    earlier = jnp.cumsum(chosen, axis=0) - chosen
    slot_hot = (earlier[:, :, None] == jnp.arange(capacity, dtype=jnp.int32)[None, None, :]).astype(
        jnp.int32
    )
    placed = chosen[:, :, None] * slot_hot
    picked = route_hot[:, :, :, None] * slot_hot[:, None, :, :]
    return (placed.astype(jnp.float32), picked.astype(jnp.float32))


def project_back(grad_gate, grad_up, wgate, wup):
    contract_cols = (((1,), (1,)), ((), ()))
    partial_value = lax.dot_general(
        grad_gate, wgate, contract_cols, preferred_element_type=jnp.float32
    )
    return partial_value + lax.dot_general(
        grad_up, wup, contract_cols, preferred_element_type=jnp.float32
    )


def row_sum(left, right):
    return lax.dot_general(
        left, right, (((0,), (0,)), ((), ())), preferred_element_type=jnp.float32
    )


def on_device(
    tokens, grad_out, expert_ids, gate_weights, gate_codes, up_codes, down_codes, block_scales
):
    experts = lax.axis_size("eg")
    width = tokens.shape[1]
    capacity = 2 * tokens.shape[0] * TOPK // experts
    placed, picked = routing_tables(expert_ids, experts, capacity)
    placed_low = placed.astype(jnp.bfloat16)
    both = jnp.concatenate([tokens, grad_out], axis=1)
    send_rows = jnp.einsum(
        "tec,td->ecd", placed_low, both, preferred_element_type=jnp.float32
    ).astype(jnp.bfloat16)
    send_gates = jnp.einsum(
        "tkec,tk->ec", picked, gate_weights.astype(jnp.float32), precision=lax.Precision.HIGHEST
    ).astype(jnp.bfloat16)
    gate_block = jnp.pad(send_gates[:, :, None], ((0, 0), (0, 0), (0, LANE - 1)))
    send = jnp.concatenate([send_rows, gate_block], axis=2)
    recv = lax.all_to_all(send, "eg", split_axis=0, concat_axis=0, tiled=True)
    recv = recv.reshape(experts * capacity, recv.shape[2])
    wgate = dequantize(gate_codes[0], block_scales[0, 0])
    wup = dequantize(up_codes[0], block_scales[0, 1])
    wdown = dequantize(down_codes[0], block_scales[0, 2])
    hid = wgate.shape[1]
    wboth = jnp.concatenate([wgate, wup], axis=1)
    wboth_ext = jnp.pad(wboth, ((0, LANE), (0, 0)))
    gathered = lax.all_gather(recv, BLK, axis=0, tiled=True)
    feats = gathered[:, :width]
    cotan = gathered[:, width : 2 * width]
    gates = gathered[:, 2 * width].astype(jnp.float32)
    both_pre = jnp.dot(feats, wboth, preferred_element_type=jnp.float32)
    gate_pre = both_pre[:, :hid]
    up_pre = both_pre[:, hid:]
    down_back = jnp.dot(cotan, wdown, preferred_element_type=jnp.float32)
    hidden, grad_gate, grad_up, gated_hidden = backward_math(gate_pre, up_pre, down_back, gates)
    grad_both = jnp.concatenate([grad_gate, grad_up], axis=1)
    back = lax.dot_general(
        grad_both, wboth_ext, (((1,), (1,)), ((), ())), preferred_element_type=jnp.float32
    )
    scores = jnp.sum(hidden * down_back, axis=1).astype(jnp.bfloat16).astype(jnp.float32)
    column = lax.broadcasted_iota(jnp.int32, back.shape, 1)
    partial_rows = jnp.where(column == width, scores[:, None], back).astype(jnp.bfloat16)
    chips = lax.axis_size("chip")
    core = lax.axis_index("core")
    by_core = partial_rows.reshape(chips, 2, -1, partial_rows.shape[1])
    mine = jnp.where(core == 0, by_core[:, 0], by_core[:, 1])
    theirs = jnp.where(core == 0, by_core[:, 1], by_core[:, 0])
    swapped = lax.ppermute(theirs, "core", [(0, 1), (1, 0)])
    pair = (mine.astype(jnp.float32) + swapped.astype(jnp.float32)).astype(jnp.bfloat16)
    pair = pair.reshape(-1, partial_rows.shape[1])
    summed = lax.psum_scatter(pair, "chip", scatter_dimension=0, tiled=True)
    both_grad = row_sum(feats, grad_both).astype(jnp.bfloat16)
    gate_grad = both_grad[None, :, :hid]
    up_grad = both_grad[None, :, hid:]
    down_grad = row_sum(cotan, gated_hidden).astype(jnp.bfloat16)[None]
    summed, gate_grad, up_grad, down_grad = lax.optimization_barrier(
        (summed, gate_grad, up_grad, down_grad)
    )
    summed = summed.reshape(experts, capacity, summed.shape[1])
    home = lax.all_to_all(summed, "eg", split_axis=0, concat_axis=0, tiled=True)
    grad_tokens = jnp.einsum(
        "tec,ecd->td", placed_low, home[:, :, :width], preferred_element_type=jnp.float32
    ).astype(jnp.bfloat16)
    grad_gates = jnp.einsum(
        "tkec,ec->tk",
        picked,
        home[:, :, width].astype(jnp.float32),
        precision=lax.Precision.HIGHEST,
    ).astype(jnp.bfloat16)
    return (grad_tokens, grad_gates, gate_grad, up_grad, down_grad)


def solution(mesh):
    n_eg, n_blk = mesh.devices.shape
    split = Mesh(mesh.devices.reshape(n_eg, n_blk // 2, 2), ("eg",) + BLK)
    in_specs = (
        P(("eg",) + BLK, None),
        P(("eg",) + BLK, None),
        P(("eg",) + BLK, None),
        P(("eg",) + BLK, None),
        P("eg", None, BLK),
        P("eg", None, BLK),
        P("eg", None, BLK),
        P("eg", None, BLK, None),
    )
    out_specs = (
        P(("eg",) + BLK, None),
        P(("eg",) + BLK, None),
        P("eg", None, BLK),
        P("eg", None, BLK),
        P("eg", None, BLK),
    )
    return jax.shard_map(
        on_device, mesh=split, in_specs=in_specs, out_specs=out_specs, check_vma=False
    )
```

```python
import jax
import jax.numpy as jnp
from jax import lax
from jax.sharding import Mesh
from jax.sharding import PartitionSpec as P

QBLOCK = 128
TOPK = 2
LANE = 128
BLK = ("chip", "core")


def dequantize(codes, scales):
    rows_in, cols_in = codes.shape
    blocks = codes.astype(jnp.float32).reshape(rows_in // QBLOCK, QBLOCK, cols_in // QBLOCK, QBLOCK)
    scaled = blocks * jnp.transpose(scales.astype(jnp.float32))[:, None, :, None]
    return scaled.reshape(rows_in, cols_in).astype(jnp.bfloat16)


def backward_math(gate_pre, up_pre, down_back, gates):
    sigma = jax.nn.sigmoid(gate_pre)
    hidden = gate_pre * sigma * up_pre
    grad_hidden = gates[:, None] * down_back
    grad_up = (grad_hidden * gate_pre * sigma).astype(jnp.bfloat16)
    grad_gate = (grad_hidden * up_pre * sigma * (1.0 + gate_pre * (1.0 - sigma))).astype(
        jnp.bfloat16
    )
    gated_hidden = (gates[:, None] * hidden).astype(jnp.bfloat16)
    return (hidden, grad_gate, grad_up, gated_hidden)


def routing_tables(expert_ids, experts, capacity):
    route_hot = (
        expert_ids[:, :, None] == jnp.arange(experts, dtype=jnp.int32)[None, None, :]
    ).astype(jnp.int32)
    chosen = jnp.sum(route_hot, axis=1)
    earlier = jnp.cumsum(chosen, axis=0) - chosen
    slot_hot = (earlier[:, :, None] == jnp.arange(capacity, dtype=jnp.int32)[None, None, :]).astype(
        jnp.int32
    )
    placed = chosen[:, :, None] * slot_hot
    picked = route_hot[:, :, :, None] * slot_hot[:, None, :, :]
    return (placed.astype(jnp.float32), picked.astype(jnp.float32))


def project_back(grad_gate, grad_up, wgate, wup):
    contract_cols = (((1,), (1,)), ((), ()))
    partial_value = lax.dot_general(
        grad_gate, wgate, contract_cols, preferred_element_type=jnp.float32
    )
    return partial_value + lax.dot_general(
        grad_up, wup, contract_cols, preferred_element_type=jnp.float32
    )


def row_sum(left, right):
    return lax.dot_general(
        left, right, (((0,), (0,)), ((), ())), preferred_element_type=jnp.float32
    )


def on_device(
    tokens, grad_out, expert_ids, gate_weights, gate_codes, up_codes, down_codes, block_scales
):
    experts = lax.axis_size("eg")
    width = tokens.shape[1]
    capacity = 2 * tokens.shape[0] * TOPK // experts
    placed, picked = routing_tables(expert_ids, experts, capacity)
    placed_low = placed.astype(jnp.bfloat16)
    both = jnp.concatenate([tokens, grad_out], axis=1)
    send_rows = jnp.einsum(
        "tec,td->ecd", placed_low, both, preferred_element_type=jnp.float32
    ).astype(jnp.bfloat16)
    send_gates = jnp.einsum(
        "tkec,tk->ec", picked, gate_weights.astype(jnp.float32), precision=lax.Precision.HIGHEST
    ).astype(jnp.bfloat16)
    gate_block = jnp.pad(send_gates[:, :, None], ((0, 0), (0, 0), (0, LANE - 1)))
    send = jnp.concatenate([send_rows, gate_block], axis=2)
    recv = lax.all_to_all(send, "eg", split_axis=0, concat_axis=0, tiled=True)
    recv = recv.reshape(experts * capacity, recv.shape[2])
    wgate = dequantize(gate_codes[0], block_scales[0, 0])
    wup = dequantize(up_codes[0], block_scales[0, 1])
    wdown = dequantize(down_codes[0], block_scales[0, 2])
    hid = wgate.shape[1]
    wboth = jnp.concatenate([wgate, wup], axis=1)
    wboth_ext = jnp.pad(wboth, ((0, LANE), (0, 0)))
    gathered = lax.all_gather(recv, BLK, axis=0, tiled=True)
    feats = gathered[:, :width]
    cotan = gathered[:, width : 2 * width]
    gates = gathered[:, 2 * width].astype(jnp.float32)
    both_pre = jnp.dot(feats, wboth, preferred_element_type=jnp.float32)
    gate_pre = both_pre[:, :hid]
    up_pre = both_pre[:, hid:]
    down_back = jnp.dot(cotan, wdown, preferred_element_type=jnp.float32)
    hidden, grad_gate, grad_up, gated_hidden = backward_math(gate_pre, up_pre, down_back, gates)
    grad_both = jnp.concatenate([grad_gate, grad_up], axis=1)
    back = lax.dot_general(
        grad_both, wboth_ext, (((1,), (1,)), ((), ())), preferred_element_type=jnp.float32
    )
    scores = jnp.sum(hidden * down_back, axis=1).astype(jnp.bfloat16).astype(jnp.float32)
    column = lax.broadcasted_iota(jnp.int32, back.shape, 1)
    partial_rows = jnp.where(column == width, scores[:, None], back).astype(jnp.bfloat16)
    chips = lax.axis_size("chip")
    core = lax.axis_index("core")
    by_core = partial_rows.reshape(chips, 2, -1, partial_rows.shape[1])
    mine = jnp.where(core == 0, by_core[:, 0], by_core[:, 1])
    theirs = jnp.where(core == 0, by_core[:, 1], by_core[:, 0])
    swapped = lax.ppermute(theirs, "core", [(0, 1), (1, 0)])
    down_grad = row_sum(cotan, gated_hidden).astype(jnp.bfloat16)[None]
    swapped, down_grad = lax.optimization_barrier((swapped, down_grad))
    pair = (mine.astype(jnp.float32) + swapped.astype(jnp.float32)).astype(jnp.bfloat16)
    pair = pair.reshape(-1, partial_rows.shape[1])
    summed = lax.psum_scatter(pair, "chip", scatter_dimension=0, tiled=True)
    both_grad = row_sum(feats, grad_both).astype(jnp.bfloat16)
    gate_grad = both_grad[None, :, :hid]
    up_grad = both_grad[None, :, hid:]
    summed, gate_grad, up_grad, down_grad = lax.optimization_barrier(
        (summed, gate_grad, up_grad, down_grad)
    )
    summed = summed.reshape(experts, capacity, summed.shape[1])
    home = lax.all_to_all(summed, "eg", split_axis=0, concat_axis=0, tiled=True)
    grad_tokens = jnp.einsum(
        "tec,ecd->td", placed_low, home[:, :, :width], preferred_element_type=jnp.float32
    ).astype(jnp.bfloat16)
    grad_gates = jnp.einsum(
        "tkec,ec->tk",
        picked,
        home[:, :, width].astype(jnp.float32),
        precision=lax.Precision.HIGHEST,
    ).astype(jnp.bfloat16)
    return (grad_tokens, grad_gates, gate_grad, up_grad, down_grad)


def solution(mesh):
    n_eg, n_blk = mesh.devices.shape
    split = Mesh(mesh.devices.reshape(n_eg, n_blk // 2, 2), ("eg",) + BLK)
    in_specs = (
        P(("eg",) + BLK, None),
        P(("eg",) + BLK, None),
        P(("eg",) + BLK, None),
        P(("eg",) + BLK, None),
        P("eg", None, BLK),
        P("eg", None, BLK),
        P("eg", None, BLK),
        P("eg", None, BLK, None),
    )
    out_specs = (
        P(("eg",) + BLK, None),
        P(("eg",) + BLK, None),
        P("eg", None, BLK),
        P("eg", None, BLK),
        P("eg", None, BLK),
    )
    return jax.shard_map(
        on_device, mesh=split, in_specs=in_specs, out_specs=out_specs, check_vma=False
    )
```

```python
import jax
import jax.numpy as jnp
from jax import lax
from jax.sharding import Mesh
from jax.sharding import PartitionSpec as P

QBLOCK = 128
TOPK = 2
LANE = 128
BLK = ("chip", "core")


def dequantize(codes, scales):
    rows_in, cols_in = codes.shape
    blocks = codes.astype(jnp.float32).reshape(rows_in // QBLOCK, QBLOCK, cols_in // QBLOCK, QBLOCK)
    scaled = blocks * jnp.transpose(scales.astype(jnp.float32))[:, None, :, None]
    return scaled.reshape(rows_in, cols_in).astype(jnp.bfloat16)


def backward_math(gate_pre, up_pre, down_back, gates):
    sigma = jax.nn.sigmoid(gate_pre)
    hidden = gate_pre * sigma * up_pre
    grad_hidden = gates[:, None] * down_back
    grad_up = (grad_hidden * gate_pre * sigma).astype(jnp.bfloat16)
    grad_gate = (grad_hidden * up_pre * sigma * (1.0 + gate_pre * (1.0 - sigma))).astype(
        jnp.bfloat16
    )
    gated_hidden = (gates[:, None] * hidden).astype(jnp.bfloat16)
    return (hidden, grad_gate, grad_up, gated_hidden)


def routing_tables(expert_ids, experts, capacity):
    route_hot = (
        expert_ids[:, :, None] == jnp.arange(experts, dtype=jnp.int32)[None, None, :]
    ).astype(jnp.int32)
    chosen = jnp.sum(route_hot, axis=1)
    earlier = jnp.cumsum(chosen, axis=0) - chosen
    slot_hot = (earlier[:, :, None] == jnp.arange(capacity, dtype=jnp.int32)[None, None, :]).astype(
        jnp.int32
    )
    placed = chosen[:, :, None] * slot_hot
    picked = route_hot[:, :, :, None] * slot_hot[:, None, :, :]
    return (placed.astype(jnp.float32), picked.astype(jnp.float32))


def project_back(grad_gate, grad_up, wgate, wup):
    contract_cols = (((1,), (1,)), ((), ()))
    partial_value = lax.dot_general(
        grad_gate, wgate, contract_cols, preferred_element_type=jnp.float32
    )
    return partial_value + lax.dot_general(
        grad_up, wup, contract_cols, preferred_element_type=jnp.float32
    )


def row_sum(left, right):
    return lax.dot_general(
        left, right, (((0,), (0,)), ((), ())), preferred_element_type=jnp.float32
    )


def on_device(
    tokens, grad_out, expert_ids, gate_weights, gate_codes, up_codes, down_codes, block_scales
):
    experts = lax.axis_size("eg")
    width = tokens.shape[1]
    capacity = 2 * tokens.shape[0] * TOPK // experts
    placed, picked = routing_tables(expert_ids, experts, capacity)
    placed_low = placed.astype(jnp.bfloat16)
    both = jnp.concatenate([tokens, grad_out], axis=1)
    send_rows = jnp.einsum(
        "tec,td->ecd", placed_low, both, preferred_element_type=jnp.float32
    ).astype(jnp.bfloat16)
    send_gates = jnp.einsum(
        "tkec,tk->ec", picked, gate_weights.astype(jnp.float32), precision=lax.Precision.HIGHEST
    ).astype(jnp.bfloat16)
    gate_block = jnp.pad(send_gates[:, :, None], ((0, 0), (0, 0), (0, LANE - 1)))
    send = jnp.concatenate([send_rows, gate_block], axis=2)
    recv = lax.all_to_all(send, "eg", split_axis=0, concat_axis=0, tiled=True)
    recv = recv.reshape(experts * capacity, recv.shape[2])
    wgate = dequantize(gate_codes[0], block_scales[0, 0])
    wup = dequantize(up_codes[0], block_scales[0, 1])
    wdown = dequantize(down_codes[0], block_scales[0, 2])
    hid = wgate.shape[1]
    wboth = jnp.concatenate([wgate, wup], axis=1)
    wboth_ext = jnp.pad(wboth, ((0, LANE), (0, 0)))
    gathered = lax.all_gather(recv, ("core", "chip"), axis=0, tiled=True)
    half = gathered.shape[0] // 2
    core = lax.axis_index("core")

    def rows_of(index):
        block = lax.dynamic_slice_in_dim(gathered, index * half, half, axis=0)
        feats = block[:, :width]
        cotan = block[:, width : 2 * width]
        gates = block[:, 2 * width].astype(jnp.float32)
        both_pre = jnp.dot(feats, wboth, preferred_element_type=jnp.float32)
        down_back = jnp.dot(cotan, wdown, preferred_element_type=jnp.float32)
        hidden, grad_gate, grad_up, gated_hidden = backward_math(
            both_pre[:, :hid], both_pre[:, hid:], down_back, gates
        )
        grad_both = jnp.concatenate([grad_gate, grad_up], axis=1)
        back = lax.dot_general(
            grad_both, wboth_ext, (((1,), (1,)), ((), ())), preferred_element_type=jnp.float32
        )
        scores = jnp.sum(hidden * down_back, axis=1).astype(jnp.bfloat16).astype(jnp.float32)
        column = lax.broadcasted_iota(jnp.int32, back.shape, 1)
        partial_rows = jnp.where(column == width, scores[:, None], back).astype(jnp.bfloat16)
        grads = (row_sum(feats, grad_both), row_sum(cotan, gated_hidden))
        return partial_rows, grads

    theirs, grads_theirs = rows_of(1 - core)
    swapped = lax.ppermute(theirs, "core", [(0, 1), (1, 0)])
    mine, grads_mine = rows_of(core)
    pair = (mine.astype(jnp.float32) + swapped.astype(jnp.float32)).astype(jnp.bfloat16)
    summed = lax.psum_scatter(pair, "chip", scatter_dimension=0, tiled=True)
    both_grad = (grads_theirs[0] + grads_mine[0]).astype(jnp.bfloat16)
    gate_grad = both_grad[None, :, :hid]
    up_grad = both_grad[None, :, hid:]
    down_grad = (grads_theirs[1] + grads_mine[1]).astype(jnp.bfloat16)[None]
    summed, gate_grad, up_grad, down_grad = lax.optimization_barrier(
        (summed, gate_grad, up_grad, down_grad)
    )
    summed = summed.reshape(experts, capacity, summed.shape[1])
    home = lax.all_to_all(summed, "eg", split_axis=0, concat_axis=0, tiled=True)
    grad_tokens = jnp.einsum(
        "tec,ecd->td", placed_low, home[:, :, :width], preferred_element_type=jnp.float32
    ).astype(jnp.bfloat16)
    grad_gates = jnp.einsum(
        "tkec,ec->tk",
        picked,
        home[:, :, width].astype(jnp.float32),
        precision=lax.Precision.HIGHEST,
    ).astype(jnp.bfloat16)
    return (grad_tokens, grad_gates, gate_grad, up_grad, down_grad)


def solution(mesh):
    n_eg, n_blk = mesh.devices.shape
    split = Mesh(mesh.devices.reshape(n_eg, n_blk // 2, 2), ("eg",) + BLK)
    in_specs = (
        P(("eg",) + BLK, None),
        P(("eg",) + BLK, None),
        P(("eg",) + BLK, None),
        P(("eg",) + BLK, None),
        P("eg", None, BLK),
        P("eg", None, BLK),
        P("eg", None, BLK),
        P("eg", None, BLK, None),
    )
    out_specs = (
        P(("eg",) + BLK, None),
        P(("eg",) + BLK, None),
        P("eg", None, BLK),
        P("eg", None, BLK),
        P("eg", None, BLK),
    )
    return jax.shard_map(
        on_device, mesh=split, in_specs=in_specs, out_specs=out_specs, check_vma=False
    )
```
